128 devices in a mesh: blk: 8 (over y, x_hi), terms: 16 (over z, x_lo, core).
Axes of the slice: x: 4 (x_hi: 2, x_lo: 2; x = x_hi * 2 + x_lo), y: 4, z: 4, core: 2. Of those that a mesh axis runs over, the one named last changes fastest.
Arguments:
- wavefunction: bfloat16 [16, 256, 256], P('blk'), may hold values from -6 to 6
- left_terms: bfloat16 [8192, 256, 256], P(('blk', 'terms')), may hold values from -0.375 to 0.375
- right_terms: bfloat16 [8192, 256, 256], P(('blk', 'terms')), may hold values from -0.015625 to 0.015625
- term_slab: int32 [8192, 1], P(('blk', 'terms')), may hold values from 0 to 7; in each aligned block of 64 rows (0 to 63, 64 to 127, ...) at most 32 rows name the same one
- term_sector: int32 [8192], P(('blk', 'terms')), may hold values from 0 to 1
- term_target: int32 [8192], P(('blk', 'terms')), may hold values from 0 to 15
Outputs:
- sigma: float32 [4096, 256], P(('blk', 'terms'))
The draws below stay inside these ranges and needn't reach their ends.
Inputs may be any that keep to these rules, and one draw needn't show every extreme that they name: `term_slab`: of the 64 terms of one device at most 32 name the same slab.
All inputs are finite; a program needn't handle non-finite values.
Results may differ from the reference program's by a relative error of at most 0.0029.
Values may be sent and summed in bfloat16 or wider, within the bound.
No kernel may reach another device: no remote copies, remote signals or barrier semaphores. Data moves between devices by JAX's collectives and lax.ppermute only.
A program may use at most 256 MiB of HBM per device.

```python
import math
import jax
import jax.numpy as jnp
import numpy as np
from jax import lax

SB = 256
SEC_DEV = 2
TERM_DEV = 64
CAP = 32
SECTORS = 16
TERMS = 8192


def with_ends(result, own_key, smallest, high):
    extent = result.shape
    place = [jax.random.randint(jax.random.fold_in(own_key, axis), (), 0, extent[axis]) for axis in range(len(extent))]
    result = result.at[tuple(place)].set(smallest)
    longest = extent.index(max(extent))
    place[longest] = (place[longest] + 1) % extent[longest]
    return result.at[tuple(place)].set(high)


def block_levels(own_key, dims, split, smallest, largest):
    def one(position, parts):
        steps = jax.random.uniform(jax.random.fold_in(jax.random.fold_in(own_key, 6), position), (parts,), jnp.float32, smallest / len(split), largest / len(split))
        return jnp.repeat(jnp.exp(steps), dims[position] // parts).reshape((-1,) + (1,) * (len(dims) - position - 1))

    factor_of = one(*split[0])
    for cut in split[1:]:
        factor_of = factor_of * one(*cut)
    return factor_of


def routed_block(own_key, own, number, rows, amount, top, most, skew):
    ranking = jax.random.permutation(own_key, amount)
    crowded, ordinary = shares(amount, rows * top, most, skew, True), shares(amount, rows * top, most, skew, False)
    places = jnp.arange(amount)

    def named(tallies, rotation):
        used = int((tallies > 0).sum())
        fixed = max(1, used // 4)
        moved = fixed + (places - fixed + rotation * (used - fixed)) % max(1, amount - fixed)
        return jnp.zeros((amount,), jnp.int32).at[ranking[jnp.where(places < fixed, places, moved)]].set(jnp.asarray(tallies, jnp.int32))

    tallies = jnp.where(number % 4 == 0, named(crowded, number // 4), named(ordinary, number - number // 4 - 1))
    mixed = jax.random.permutation(jax.random.fold_in(own, 3), amount)
    source_of, sink = mixed[0:amount // 2 * 2:2], mixed[1:amount // 2 * 2:2]
    slack = jnp.minimum(tallies[source_of] - 1, most - tallies[sink]) // 2
    slack = jnp.where((source_of == ranking[0]) | (sink == ranking[0]) | (tallies[sink] == 0), 0, jnp.maximum(slack, 0))
    moved = jax.random.randint(jax.random.fold_in(own, 4), (amount // 2,), 0, 1 << 20) % (slack + 1)
    tallies = tallies.at[source_of].add(-moved).at[sink].add(moved)
    members = jnp.searchsorted(jnp.cumsum(tallies), jnp.arange(rows * top), side="right").astype(jnp.int32)
    grid = members.reshape(top, rows).T
    grid = grid[jax.random.permutation(jax.random.fold_in(own, 1), rows)]
    rotation = jax.random.randint(jax.random.fold_in(own, 2), (rows, 1), 0, top)
    return jnp.take_along_axis(grid, (jnp.arange(top)[None, :] + rotation) % top, axis=1)


def shares(amount, total, most, skew, full):
    portions = [(1 << 20) // math.isqrt(rank ** skew) + 1 for rank in range(1, amount + 1)]
    largest = most if full else min(most, max(-(-total // amount), total * portions[0] // sum(portions)))
    least = 1 if total - largest >= amount - 1 else 0
    holding, spare = [largest] + [least] * (amount - 1), total - largest - least * (amount - 1)
    while spare > 0:
        candidates = [i for i in range(1, amount) if holding[i] < largest] or [i for i in range(1, amount) if holding[i] < most]
        whole, remaining = sum([portions[i] for i in candidates]), spare
        for i in candidates:
            addition = min(most - holding[i], max(1, remaining * portions[i] // whole), spare)
            holding[i] = holding[i] + addition
            spare = spare - addition
    return np.array(holding)


def scatter_about(own_key, shape, width, reach, split=(), held_as=jnp.bfloat16):
    entries = jax.random.normal(own_key, shape, jnp.float32) * width
    if len(split) > 0:
        entries = block_levels(own_key, shape, split, -0.22, 0.18) * entries
    return jnp.clip(entries, min=-reach, max=reach).astype(held_as)


def setup_inputs(seed: int = 0) -> dict:
    streams_of = jax.random.split(jax.random.key(seed), 7)
    wavefunction = scatter_about(streams_of[0], (SECTORS, SB, SB), 1.0, 6.0, ((0, 8),))
    left_terms = scatter_about(streams_of[1], (TERMS, SB, SB), SB ** -0.5, 0.375, ((0, 128),))
    right_terms = scatter_about(streams_of[2], (TERMS, SB, SB), (SB * TERMS // SECTORS) ** -0.5, 0.015625, ((0, 128),))
    term_slab_keys = jax.random.split(jax.random.fold_in(streams_of[3], 1), TERMS // TERM_DEV)
    term_slab_turns = jax.random.permutation(jax.random.fold_in(streams_of[3], 3), TERMS // TERM_DEV)
    term_slab = jax.vmap(lambda own, number: routed_block(jax.random.fold_in(streams_of[3], 2), own, number, TERM_DEV, SECTORS // SEC_DEV, 1, CAP, 2))(term_slab_keys, term_slab_turns).reshape((TERMS, 1))
    term_sector = with_ends(jax.random.randint(streams_of[4], (TERMS,), 0, SEC_DEV), jax.random.fold_in(streams_of[4], 1), 0, SEC_DEV - 1).astype(jnp.int32)
    term_target = with_ends(jax.random.randint(streams_of[5], (TERMS,), 0, SECTORS), jax.random.fold_in(streams_of[5], 1), 0, SECTORS - 1).astype(jnp.int32)
    return {"wavefunction": wavefunction, "left_terms": left_terms, "right_terms": right_terms, "term_slab": term_slab, "term_sector": term_sector, "term_target": term_target}


def reference(wavefunction, left_terms, right_terms, term_slab, term_sector, term_target):
    sources = (term_slab[:, 0] * SEC_DEV + term_sector).astype(jnp.int32)
    groups = TERMS // TERM_DEV

    def one_group(running, packed):
        left_block, right_block, group_sources, targets = packed
        psi_blocks = wavefunction[group_sources].astype(jnp.float32)
        left_part = jnp.einsum("tij,tjk->tik", left_block.astype(jnp.float32), psi_blocks, precision=lax.Precision.HIGHEST)
        left_part = lax.optimization_barrier(left_part.astype(jnp.bfloat16)).astype(jnp.float32)
        term_image = jnp.einsum("tik,tlk->til", left_part, right_block.astype(jnp.float32), precision=lax.Precision.HIGHEST)
        return running.at[targets].add(term_image), None

    packed = (left_terms.reshape(groups, TERM_DEV, SB, SB), right_terms.reshape(groups, TERM_DEV, SB, SB), sources.reshape(groups, TERM_DEV), term_target.reshape(groups, TERM_DEV))
    running, unused = lax.scan(one_group, jnp.zeros((SECTORS, SB, SB), jnp.float32), packed)
    return running.reshape(SECTORS * SB, SB)
```

```python
import jax
import jax.numpy as jnp
from jax import lax
from jax.sharding import Mesh
from jax.sharding import PartitionSpec as P

PHYS = ("y", "xh", "z", "xl", "c")


def add_terms(running, wave_blocks, left_block, right_block, local_rows, targets):
    psi_blocks = wave_blocks[local_rows]
    left_part = jnp.einsum(
        "tij,tjk->tik", left_block, psi_blocks, preferred_element_type=jnp.float32
    ).astype(jnp.bfloat16)
    term_image = jnp.einsum(
        "tik,tlk->til", left_part, right_block, preferred_element_type=jnp.float32
    )
    return running.at[targets].add(term_image)


def gather_blocks(wavefunction, n_blk):
    copies = jnp.broadcast_to(wavefunction[None], (n_blk,) + wavefunction.shape)
    got = lax.all_to_all(copies, ("y", "xh"), 0, 0, tiled=True)
    return got.reshape((-1,) + wavefunction.shape[1:])


def reduce_rows(stacked, n_core, n_rest):
    rows = stacked.shape[0] // (n_core * n_rest)
    y = stacked.reshape(n_rest, n_core, rows, stacked.shape[1]).transpose(1, 0, 2, 3)
    y = lax.all_to_all(y, "c", 0, 0, tiled=True).reshape(n_core, n_rest, rows, -1).sum(0)
    y = lax.all_to_all(y, ("y", "xh", "z", "xl"), 0, 0, tiled=True)
    return y.reshape(n_rest, rows, -1).sum(0)


def on_device(wavefunction, left_terms, right_terms, term_slab, term_sector, term_target):
    per_slab = wavefunction.shape[0]
    n_blk = lax.axis_size(("y", "xh"))
    n_core = lax.axis_size("c")
    n_rest = lax.axis_size(("y", "xh", "z", "xl"))
    sectors = per_slab * n_blk
    block_width = wavefunction.shape[1]
    slab_index = term_slab[:, 0]
    partial_value = jnp.zeros((sectors, block_width, block_width), jnp.float32)
    gathered = gather_blocks(wavefunction, n_blk)
    partial_value = add_terms(
        partial_value,
        gathered,
        left_terms,
        right_terms,
        slab_index * per_slab + term_sector,
        term_target,
    )
    stacked = partial_value.reshape(sectors * block_width, block_width)
    return reduce_rows(stacked, n_core, n_rest)


def solution(mesh):
    blk, terms = mesh.axis_names
    n_blk, n_terms = mesh.shape[blk], mesh.shape[terms]
    n_core = 2
    phys = Mesh(
        mesh.devices.reshape(n_blk // 2, 2, n_terms // (2 * n_core), 2, n_core), PHYS
    )
    wave = ("y", "xh")
    spread = PHYS
    placed = (
        P(wave, None, None),
        P(spread, None, None),
        P(spread, None, None),
        P(spread, None),
        P(spread),
        P(spread),
    )
    return jax.shard_map(
        on_device, mesh=phys, in_specs=placed, out_specs=P(spread, None), check_vma=False
    )
```

```python
import jax
import jax.numpy as jnp
from jax import lax
from jax.experimental import pallas as pl
from jax.experimental.pallas import tpu as pltpu
from jax.sharding import Mesh
from jax.sharding import PartitionSpec as P

PHYS = ("y", "xh", "z", "xl", "c")
TERM_BLOCK = 8


def sigma_kernel(src_ref, tgt_ref, psi_ref, left_ref, right_ref, out_ref):
    step = pl.program_id(0)

    @pl.when(step == 0)
    def _():
        out_ref[...] = jnp.zeros_like(out_ref)

    for j in range(TERM_BLOCK):
        t = step * TERM_BLOCK + j
        left_part = jnp.dot(
            left_ref[j], psi_ref[src_ref[t]], preferred_element_type=jnp.float32
        ).astype(jnp.bfloat16)
        term_image = lax.dot_general(
            left_part, right_ref[j], (((1,), (1,)), ((), ())),
            preferred_element_type=jnp.float32,
        )
        out_ref[tgt_ref[t]] += term_image


def add_terms(wave_blocks, left_terms, right_terms, sources, targets):
    sectors, width, _ = wave_blocks.shape
    n_terms = left_terms.shape[0]
    whole = pl.BlockSpec((sectors, width, width), lambda i, s, g: (0, 0, 0))
    per_step = pl.BlockSpec((TERM_BLOCK, width, width), lambda i, s, g: (i, 0, 0))
    return pl.pallas_call(
        sigma_kernel,
        out_shape=jax.ShapeDtypeStruct((sectors, width, width), jnp.float32),
        grid_spec=pltpu.PrefetchScalarGridSpec(
            num_scalar_prefetch=2,
            grid=(n_terms // TERM_BLOCK,),
            in_specs=[whole, per_step, per_step],
            out_specs=whole,
        ),
        compiler_params=pltpu.CompilerParams(dimension_semantics=("arbitrary",)),
    )(sources, targets, wave_blocks, left_terms, right_terms)


def gather_blocks(wavefunction, n_blk):
    copies = jnp.broadcast_to(wavefunction[None], (n_blk,) + wavefunction.shape)
    got = lax.all_to_all(copies, ("y", "xh"), 0, 0, tiled=True)
    return got.reshape((-1,) + wavefunction.shape[1:])


def reduce_rows(stacked, n_core, n_rest):
    rows = stacked.shape[0] // (n_core * n_rest)
    y = stacked.reshape(n_rest, n_core, rows, stacked.shape[1]).transpose(1, 0, 2, 3)
    y = lax.all_to_all(y, "c", 0, 0, tiled=True).reshape(n_core, n_rest, rows, -1).sum(0)
    y = lax.all_to_all(y, ("y", "xh", "z", "xl"), 0, 0, tiled=True)
    return y.reshape(n_rest, rows, -1).sum(0)


def on_device(wavefunction, left_terms, right_terms, term_slab, term_sector, term_target):
    per_slab = wavefunction.shape[0]
    n_blk = lax.axis_size(("y", "xh"))
    n_core = lax.axis_size("c")
    n_rest = lax.axis_size(("y", "xh", "z", "xl"))
    sectors = per_slab * n_blk
    block_width = wavefunction.shape[1]
    sources = term_slab[:, 0] * per_slab + term_sector
    gathered = gather_blocks(wavefunction, n_blk)
    partial_value = add_terms(gathered, left_terms, right_terms, sources, term_target)
    stacked = partial_value.reshape(sectors * block_width, block_width)
    return reduce_rows(stacked, n_core, n_rest)


def solution(mesh):
    blk, terms = mesh.axis_names
    n_blk, n_terms = mesh.shape[blk], mesh.shape[terms]
    n_core = 2
    phys = Mesh(
        mesh.devices.reshape(n_blk // 2, 2, n_terms // (2 * n_core), 2, n_core), PHYS
    )
    wave = ("y", "xh")
    spread = PHYS
    placed = (
        P(wave, None, None),
        P(spread, None, None),
        P(spread, None, None),
        P(spread, None),
        P(spread),
        P(spread),
    )
    return jax.shard_map(
        on_device, mesh=phys, in_specs=placed, out_specs=P(spread, None), check_vma=False
    )
```

```python
import jax
import jax.numpy as jnp
from jax import lax
from jax.experimental import pallas as pl
from jax.experimental.pallas import tpu as pltpu
from jax.sharding import Mesh
from jax.sharding import PartitionSpec as P

PHYS = ("y", "xh", "z", "xl", "c")
TERM_BLOCK = 8


def sigma_kernel(src_ref, tgt_ref, psi_ref, left_ref, right_ref, out_ref):
    step = pl.program_id(0)

    @pl.when(step == 0)
    def _():
        out_ref[...] = jnp.zeros_like(out_ref)

    for j in range(TERM_BLOCK):
        t = step * TERM_BLOCK + j
        left_part = jnp.dot(
            left_ref[j], psi_ref[src_ref[t]], preferred_element_type=jnp.float32
        ).astype(jnp.bfloat16)
        term_image = lax.dot_general(
            left_part, right_ref[j], (((1,), (1,)), ((), ())),
            preferred_element_type=jnp.float32,
        )
        out_ref[tgt_ref[t]] += term_image


def add_terms(wave_blocks, left_terms, right_terms, sources, targets):
    sectors, width, _ = wave_blocks.shape
    n_terms = left_terms.shape[0]
    whole = pl.BlockSpec((sectors, width, width), lambda i, s, g: (0, 0, 0))
    per_step = pl.BlockSpec((TERM_BLOCK, width, width), lambda i, s, g: (i, 0, 0))
    return pl.pallas_call(
        sigma_kernel,
        out_shape=jax.ShapeDtypeStruct((sectors, width, width), jnp.float32),
        grid_spec=pltpu.PrefetchScalarGridSpec(
            num_scalar_prefetch=2,
            grid=(n_terms // TERM_BLOCK,),
            in_specs=[whole, per_step, per_step],
            out_specs=whole,
        ),
        compiler_params=pltpu.CompilerParams(dimension_semantics=("arbitrary",)),
    )(sources, targets, wave_blocks, left_terms, right_terms)


def gather_blocks(wavefunction, n_blk):
    core = lax.axis_index("c")
    mine = lax.dynamic_index_in_dim(wavefunction, core, 0, keepdims=False)
    copies = jnp.broadcast_to(mine[None], (n_blk,) + mine.shape)
    got = lax.all_to_all(copies, ("y", "xh"), 0, 0, tiled=True)
    other = lax.ppermute(got, "c", [(0, 1), (1, 0)])
    low = jnp.where(core == 0, got, other)
    high = jnp.where(core == 0, other, got)
    return jnp.stack([low, high], 1).reshape((-1,) + wavefunction.shape[1:])


def reduce_rows(stacked, n_core, n_rest):
    rows = stacked.shape[0] // (n_core * n_rest)
    y = stacked.reshape(n_rest, n_core, rows, stacked.shape[1])
    core = lax.axis_index("c")
    mine = jnp.where(core == 0, y[:, 0], y[:, 1])
    other = jnp.where(core == 0, y[:, 1], y[:, 0])
    y = mine + lax.ppermute(other, "c", [(0, 1), (1, 0)])
    y = lax.all_to_all(y, ("y", "xh", "z", "xl"), 0, 0, tiled=True)
    return y.sum(0)


def on_device(wavefunction, left_terms, right_terms, term_slab, term_sector, term_target):
    per_slab = wavefunction.shape[0]
    n_blk = lax.axis_size(("y", "xh"))
    n_core = lax.axis_size("c")
    n_rest = lax.axis_size(("y", "xh", "z", "xl"))
    sectors = per_slab * n_blk
    block_width = wavefunction.shape[1]
    sources = term_slab[:, 0] * per_slab + term_sector
    gathered = gather_blocks(wavefunction, n_blk)
    partial_value = add_terms(gathered, left_terms, right_terms, sources, term_target)
    stacked = partial_value.reshape(sectors * block_width, block_width)
    return reduce_rows(stacked, n_core, n_rest)


def solution(mesh):
    blk, terms = mesh.axis_names
    n_blk, n_terms = mesh.shape[blk], mesh.shape[terms]
    n_core = 2
    phys = Mesh(
        mesh.devices.reshape(n_blk // 2, 2, n_terms // (2 * n_core), 2, n_core), PHYS
    )
    wave = ("y", "xh")
    spread = PHYS
    placed = (
        P(wave, None, None),
        P(spread, None, None),
        P(spread, None, None),
        P(spread, None),
        P(spread),
        P(spread),
    )
    return jax.shard_map(
        on_device, mesh=phys, in_specs=placed, out_specs=P(spread, None), check_vma=False
    )
```

```python
import jax
import jax.numpy as jnp
from jax import lax
from jax.experimental import pallas as pl
from jax.experimental.pallas import tpu as pltpu
from jax.sharding import Mesh
from jax.sharding import PartitionSpec as P

PHYS = ("y", "xh", "z", "xl", "c")
TERM_BLOCK = 8


def sigma_kernel(core_ref, slab_ref, sector_ref, tgt_ref, own_ref, swapped_ref,
                 left_ref, right_ref, out_ref):
    step = pl.program_id(0)
    core = core_ref[0]
    n_core = out_ref.shape[0]
    bands = out_ref.shape[2]
    band = out_ref.shape[3]

    @pl.when(step == 0)
    def _():
        out_ref[...] = jnp.zeros_like(out_ref)

    for j in range(TERM_BLOCK):
        t = step * TERM_BLOCK + j
        slab = slab_ref[t]
        target = tgt_ref[t]

        def accumulate(psi_ref, j=j, slab=slab, target=target):
            left_part = jnp.dot(
                left_ref[j], psi_ref[slab], preferred_element_type=jnp.float32
            ).astype(jnp.bfloat16)
            term_image = lax.dot_general(
                left_part, right_ref[j], (((1,), (1,)), ((), ())),
                preferred_element_type=jnp.float32,
            )
            for q in range(bands):
                for cc in range(n_core):
                    row = (q * n_core + cc) * band
                    slot = jnp.where(cc == core, 0, 1)
                    out_ref[slot, target, q] += term_image[row:row + band]

        own = sector_ref[t] == core

        @pl.when(own)
        def _():
            accumulate(own_ref)

        @pl.when(jnp.logical_not(own))
        def _():
            accumulate(swapped_ref)


def add_terms(own, swapped, left_terms, right_terms, slab, sector, targets, core, n_core, band):
    n_slab, width, _ = own.shape
    sectors = n_slab * n_core
    bands = width // (band * n_core)
    n_terms = left_terms.shape[0]
    whole = pl.BlockSpec((n_slab, width, width), lambda i, *_: (0, 0, 0))
    per_step = pl.BlockSpec((TERM_BLOCK, width, width), lambda i, *_: (i, 0, 0))
    out_shape = (n_core, sectors, bands, band, width)
    return pl.pallas_call(
        sigma_kernel,
        out_shape=jax.ShapeDtypeStruct(out_shape, jnp.float32),
        grid_spec=pltpu.PrefetchScalarGridSpec(
            num_scalar_prefetch=4,
            grid=(n_terms // TERM_BLOCK,),
            in_specs=[whole, whole, per_step, per_step],
            out_specs=pl.BlockSpec(out_shape, lambda i, *_: (0,) * len(out_shape)),
        ),
        compiler_params=pltpu.CompilerParams(dimension_semantics=("arbitrary",)),
    )(core, slab, sector, targets, own, swapped, left_terms, right_terms)


def gather_blocks(wavefunction, n_blk):
    core = lax.axis_index("c")
    mine = lax.dynamic_index_in_dim(wavefunction, core, 0, keepdims=False)
    copies = jnp.broadcast_to(mine[None], (n_blk,) + mine.shape)
    own = lax.all_to_all(copies, ("y", "xh"), 0, 0, tiled=True)
    swapped = lax.ppermute(own, "c", [(0, 1), (1, 0)])
    return own, swapped


def on_device(wavefunction, left_terms, right_terms, term_slab, term_sector, term_target):
    n_blk = lax.axis_size(("y", "xh"))
    n_core = lax.axis_size("c")
    n_rest = lax.axis_size(("y", "xh", "z", "xl"))
    width = wavefunction.shape[1]
    band = wavefunction.shape[0] * n_blk * width // (n_core * n_rest)
    core = lax.axis_index("c").astype(jnp.int32).reshape(1)
    own, swapped = gather_blocks(wavefunction, n_blk)
    parts = add_terms(
        own, swapped, left_terms, right_terms, term_slab[:, 0], term_sector, term_target,
        core, n_core, band,
    )
    mine = parts[0].reshape(n_rest, band, width)
    other = parts[1].reshape(n_rest, band, width)
    summed = mine + lax.ppermute(other, "c", [(0, 1), (1, 0)])
    got = lax.all_to_all(summed, ("y", "xh", "z", "xl"), 0, 0, tiled=True)
    return got.sum(0)


def solution(mesh):
    blk, terms = mesh.axis_names
    n_blk, n_terms = mesh.shape[blk], mesh.shape[terms]
    n_core = 2
    phys = Mesh(
        mesh.devices.reshape(n_blk // 2, 2, n_terms // (2 * n_core), 2, n_core), PHYS
    )
    wave = ("y", "xh")
    spread = PHYS
    placed = (
        P(wave, None, None),
        P(spread, None, None),
        P(spread, None, None),
        P(spread, None),
        P(spread),
        P(spread),
    )
    return jax.shard_map(
        on_device, mesh=phys, in_specs=placed, out_specs=P(spread, None), check_vma=False
    )
```

```python
import jax
import jax.numpy as jnp
from jax import lax
from jax.experimental import pallas as pl
from jax.experimental.pallas import tpu as pltpu
from jax.sharding import Mesh
from jax.sharding import PartitionSpec as P

PHYS = ("y", "xh", "z", "xl", "c")
TERM_BLOCK = 32


def sigma_kernel(src_ref, tgt_ref, psi_ref, left_ref, right_ref, out_ref):
    step = pl.program_id(0)

    @pl.when(step == 0)
    def _():
        out_ref[...] = jnp.zeros_like(out_ref)

    for j in range(TERM_BLOCK):
        t = step * TERM_BLOCK + j
        left_part = jnp.dot(
            left_ref[j], psi_ref[src_ref[t]], preferred_element_type=jnp.float32
        ).astype(jnp.bfloat16)
        term_image = lax.dot_general(
            left_part, right_ref[j], (((1,), (1,)), ((), ())),
            preferred_element_type=jnp.float32,
        )
        out_ref[tgt_ref[t]] += term_image


def add_terms(wave_blocks, left_terms, right_terms, sources, targets):
    sectors, width, _ = wave_blocks.shape
    n_terms = left_terms.shape[0]
    whole = pl.BlockSpec((sectors, width, width), lambda i, s, g: (0, 0, 0))
    per_step = pl.BlockSpec((TERM_BLOCK, width, width), lambda i, s, g: (i, 0, 0))
    return pl.pallas_call(
        sigma_kernel,
        out_shape=jax.ShapeDtypeStruct((sectors, width, width), jnp.float32),
        grid_spec=pltpu.PrefetchScalarGridSpec(
            num_scalar_prefetch=2,
            grid=(n_terms // TERM_BLOCK,),
            in_specs=[whole, per_step, per_step],
            out_specs=whole,
        ),
        compiler_params=pltpu.CompilerParams(dimension_semantics=("arbitrary",)),
    )(sources, targets, wave_blocks, left_terms, right_terms)


def gather_blocks(wavefunction, n_blk):
    core = lax.axis_index("c")
    mine = lax.dynamic_index_in_dim(wavefunction, core, 0, keepdims=False)
    copies = jnp.broadcast_to(mine[None], (n_blk,) + mine.shape)
    got = lax.all_to_all(copies, ("y", "xh"), 0, 0, tiled=True)
    other = lax.ppermute(got, "c", [(0, 1), (1, 0)])
    low = jnp.where(core == 0, got, other)
    high = jnp.where(core == 0, other, got)
    return jnp.stack([low, high], 1).reshape((-1,) + wavefunction.shape[1:])


def reduce_rows(stacked, n_core, n_rest):
    rows = stacked.shape[0] // (n_core * n_rest)
    y = stacked.reshape(n_rest, n_core, rows, stacked.shape[1])
    core = lax.axis_index("c")
    mine = jnp.where(core == 0, y[:, 0], y[:, 1])
    other = jnp.where(core == 0, y[:, 1], y[:, 0])
    y = mine + lax.ppermute(other, "c", [(0, 1), (1, 0)])
    y = lax.all_to_all(y, ("y", "xh", "z", "xl"), 0, 0, tiled=True)
    return y.sum(0)


def on_device(wavefunction, left_terms, right_terms, term_slab, term_sector, term_target):
    per_slab = wavefunction.shape[0]
    n_blk = lax.axis_size(("y", "xh"))
    n_core = lax.axis_size("c")
    n_rest = lax.axis_size(("y", "xh", "z", "xl"))
    sectors = per_slab * n_blk
    block_width = wavefunction.shape[1]
    sources = term_slab[:, 0] * per_slab + term_sector
    gathered = gather_blocks(wavefunction, n_blk)
    partial_value = add_terms(gathered, left_terms, right_terms, sources, term_target)
    stacked = partial_value.reshape(sectors * block_width, block_width)
    return reduce_rows(stacked, n_core, n_rest)


def solution(mesh):
    blk, terms = mesh.axis_names
    n_blk, n_terms = mesh.shape[blk], mesh.shape[terms]
    n_core = 2
    phys = Mesh(
        mesh.devices.reshape(n_blk // 2, 2, n_terms // (2 * n_core), 2, n_core), PHYS
    )
    wave = ("y", "xh")
    spread = PHYS
    placed = (
        P(wave, None, None),
        P(spread, None, None),
        P(spread, None, None),
        P(spread, None),
        P(spread),
        P(spread),
    )
    return jax.shard_map(
        on_device, mesh=phys, in_specs=placed, out_specs=P(spread, None), check_vma=False
    )
```

```python
import jax
import jax.numpy as jnp
from jax import lax
from jax.experimental import pallas as pl
from jax.experimental.pallas import tpu as pltpu
from jax.sharding import Mesh
from jax.sharding import PartitionSpec as P

PHYS = ("y", "xh", "z", "xl", "c")
TERM_BLOCK = 32


def sigma_kernel(core_ref, src_ref, tgt_ref, psi_ref, left_ref, right_ref, out_ref):
    step = pl.program_id(0)
    rows = out_ref.shape[1]

    @pl.when(step == 0)
    def _():
        out_ref[...] = jnp.zeros_like(out_ref)

    for j in range(TERM_BLOCK):
        t = step * TERM_BLOCK + j
        left_rows = left_ref[j].reshape(rows, left_ref.shape[-1])
        left_part = jnp.dot(
            left_rows, psi_ref[src_ref[t]], preferred_element_type=jnp.float32
        ).astype(jnp.bfloat16)
        term_image = lax.dot_general(
            left_part, right_ref[j], (((1,), (1,)), ((), ())),
            preferred_element_type=jnp.float32,
        )
        out_ref[tgt_ref[t]] += term_image


def add_terms(wave_blocks, left_bands, right_terms, sources, targets, core, other):
    sectors, width, _ = wave_blocks.shape
    n_terms, bands, n_core, band, _ = left_bands.shape
    rows = bands * band

    def pick(c):
        return (c + 1) % n_core if other else c

    whole = pl.BlockSpec((sectors, width, width), lambda i, *_: (0, 0, 0))
    per_step = pl.BlockSpec((TERM_BLOCK, width, width), lambda i, *_: (i, 0, 0))
    left_step = pl.BlockSpec(
        (TERM_BLOCK, bands, None, band, width), lambda i, c, *_: (i, 0, pick(c[0]), 0, 0)
    )
    out_spec = pl.BlockSpec((sectors, rows, width), lambda i, *_: (0, 0, 0))
    return pl.pallas_call(
        sigma_kernel,
        out_shape=jax.ShapeDtypeStruct((sectors, rows, width), jnp.float32),
        grid_spec=pltpu.PrefetchScalarGridSpec(
            num_scalar_prefetch=3,
            grid=(n_terms // TERM_BLOCK,),
            in_specs=[whole, left_step, per_step],
            out_specs=out_spec,
        ),
        compiler_params=pltpu.CompilerParams(dimension_semantics=("arbitrary",)),
    )(core, sources, targets, wave_blocks, left_bands, right_terms)


def gather_blocks(wavefunction, n_blk):
    core = lax.axis_index("c")
    mine = lax.dynamic_index_in_dim(wavefunction, core, 0, keepdims=False)
    copies = jnp.broadcast_to(mine[None], (n_blk,) + mine.shape)
    got = lax.all_to_all(copies, ("y", "xh"), 0, 0, tiled=True)
    other = lax.ppermute(got, "c", [(0, 1), (1, 0)])
    low = jnp.where(core == 0, got, other)
    high = jnp.where(core == 0, other, got)
    return jnp.stack([low, high], 1).reshape((-1,) + wavefunction.shape[1:])


def on_device(wavefunction, left_terms, right_terms, term_slab, term_sector, term_target):
    per_slab = wavefunction.shape[0]
    n_blk = lax.axis_size(("y", "xh"))
    n_core = lax.axis_size("c")
    n_rest = lax.axis_size(("y", "xh", "z", "xl"))
    width = wavefunction.shape[1]
    band = per_slab * n_blk * width // (n_core * n_rest)
    bands = width // (band * n_core)
    sources = term_slab[:, 0] * per_slab + term_sector
    core = lax.axis_index("c").astype(jnp.int32).reshape(1)
    gathered = gather_blocks(wavefunction, n_blk)
    left_bands = left_terms.reshape(left_terms.shape[0], bands, n_core, band, width)
    other = add_terms(gathered, left_bands, right_terms, sources, term_target, core, True)
    sent = lax.ppermute(other.reshape(n_rest, band, width), "c", [(0, 1), (1, 0)])
    mine = add_terms(gathered, left_bands, right_terms, sources, term_target, core, False)
    summed = mine.reshape(n_rest, band, width) + sent
    got = lax.all_to_all(summed, ("y", "xh", "z", "xl"), 0, 0, tiled=True)
    return got.sum(0)


def solution(mesh):
    blk, terms = mesh.axis_names
    n_blk, n_terms = mesh.shape[blk], mesh.shape[terms]
    n_core = 2
    phys = Mesh(
        mesh.devices.reshape(n_blk // 2, 2, n_terms // (2 * n_core), 2, n_core), PHYS
    )
    wave = ("y", "xh")
    spread = PHYS
    placed = (
        P(wave, None, None),
        P(spread, None, None),
        P(spread, None, None),
        P(spread, None),
        P(spread),
        P(spread),
    )
    return jax.shard_map(
        on_device, mesh=phys, in_specs=placed, out_specs=P(spread, None), check_vma=False
    )
```

```python
import jax
import jax.numpy as jnp
from jax import lax
from jax.experimental import pallas as pl
from jax.experimental.pallas import tpu as pltpu
from jax.sharding import Mesh
from jax.sharding import PartitionSpec as P

PHYS = ("y", "xh", "z", "xl", "c")
TERM_BLOCK = 32


def sigma_kernel(core_ref, src_ref, tgt_ref, own_ref, swapped_ref, left_ref, right_ref,
                 out_ref, psi_ref):
    step = pl.program_id(0)

    @pl.when(step == 0)
    def _():
        core = core_ref[0]
        for b in range(own_ref.shape[0]):
            psi_ref[2 * b + core] = own_ref[b]
            psi_ref[2 * b + 1 - core] = swapped_ref[b]
        out_ref[...] = jnp.zeros_like(out_ref)

    for j in range(TERM_BLOCK):
        t = step * TERM_BLOCK + j
        left_part = jnp.dot(
            left_ref[j], psi_ref[src_ref[t]], preferred_element_type=jnp.float32
        ).astype(jnp.bfloat16)
        term_image = lax.dot_general(
            left_part, right_ref[j], (((1,), (1,)), ((), ())),
            preferred_element_type=jnp.float32,
        )
        out_ref[tgt_ref[t]] += term_image


def add_terms(own, swapped, left_terms, right_terms, sources, targets, core):
    n_slab, width, _ = own.shape
    sectors = 2 * n_slab
    n_terms = left_terms.shape[0]
    half = pl.BlockSpec((n_slab, width, width), lambda i, *_: (0, 0, 0))
    whole = pl.BlockSpec((sectors, width, width), lambda i, *_: (0, 0, 0))
    per_step = pl.BlockSpec((TERM_BLOCK, width, width), lambda i, *_: (i, 0, 0))
    return pl.pallas_call(
        sigma_kernel,
        out_shape=jax.ShapeDtypeStruct((sectors, width, width), jnp.float32),
        grid_spec=pltpu.PrefetchScalarGridSpec(
            num_scalar_prefetch=3,
            grid=(n_terms // TERM_BLOCK,),
            in_specs=[half, half, per_step, per_step],
            out_specs=whole,
            scratch_shapes=[pltpu.VMEM((sectors, width, width), own.dtype)],
        ),
        compiler_params=pltpu.CompilerParams(dimension_semantics=("arbitrary",)),
    )(core, sources, targets, own, swapped, left_terms, right_terms)


def gather_blocks(wavefunction, n_blk):
    core = lax.axis_index("c")
    mine = lax.dynamic_index_in_dim(wavefunction, core, 0, keepdims=False)
    copies = jnp.broadcast_to(mine[None], (n_blk,) + mine.shape)
    own = lax.all_to_all(copies, ("y", "xh"), 0, 0, tiled=True)
    swapped = lax.ppermute(own, "c", [(0, 1), (1, 0)])
    return own, swapped


def reduce_rows(stacked, n_core, n_rest):
    rows = stacked.shape[0] // (n_core * n_rest)
    y = stacked.reshape(n_rest, n_core, rows, stacked.shape[1])
    core = lax.axis_index("c")
    mine = jnp.where(core == 0, y[:, 0], y[:, 1])
    other = jnp.where(core == 0, y[:, 1], y[:, 0])
    y = mine + lax.ppermute(other, "c", [(0, 1), (1, 0)])
    y = lax.all_to_all(y, ("y", "xh", "z", "xl"), 0, 0, tiled=True)
    return y.sum(0)


def on_device(wavefunction, left_terms, right_terms, term_slab, term_sector, term_target):
    per_slab = wavefunction.shape[0]
    n_blk = lax.axis_size(("y", "xh"))
    n_core = lax.axis_size("c")
    n_rest = lax.axis_size(("y", "xh", "z", "xl"))
    sectors = per_slab * n_blk
    block_width = wavefunction.shape[1]
    sources = term_slab[:, 0] * per_slab + term_sector
    core = lax.axis_index("c").astype(jnp.int32).reshape(1)
    own, swapped = gather_blocks(wavefunction, n_blk)
    partial_value = add_terms(own, swapped, left_terms, right_terms, sources, term_target, core)
    stacked = partial_value.reshape(sectors * block_width, block_width)
    return reduce_rows(stacked, n_core, n_rest)


def solution(mesh):
    blk, terms = mesh.axis_names
    n_blk, n_terms = mesh.shape[blk], mesh.shape[terms]
    n_core = 2
    phys = Mesh(
        mesh.devices.reshape(n_blk // 2, 2, n_terms // (2 * n_core), 2, n_core), PHYS
    )
    wave = ("y", "xh")
    spread = PHYS
    placed = (
        P(wave, None, None),
        P(spread, None, None),
        P(spread, None, None),
        P(spread, None),
        P(spread),
        P(spread),
    )
    return jax.shard_map(
        on_device, mesh=phys, in_specs=placed, out_specs=P(spread, None), check_vma=False
    )
```

```python
import jax
import jax.numpy as jnp
from jax import lax
from jax.experimental import pallas as pl
from jax.experimental.pallas import tpu as pltpu
from jax.sharding import Mesh
from jax.sharding import PartitionSpec as P

PHYS = ("y", "xh", "z", "xl", "c")
TERM_BLOCK = 32


def sigma_kernel(core_ref, src_ref, tgt_ref, own_ref, swapped_ref, left_ref, right_ref,
                 out_ref, psi_ref):
    step = pl.program_id(0)

    @pl.when(step == 0)
    def _():
        core = core_ref[0]
        for b in range(own_ref.shape[0]):
            psi_ref[2 * b + core] = own_ref[b]
            psi_ref[2 * b + 1 - core] = swapped_ref[b]
        out_ref[...] = jnp.zeros_like(out_ref)

    for j in range(TERM_BLOCK):
        t = step * TERM_BLOCK + j
        left_part = jnp.dot(
            left_ref[j], psi_ref[src_ref[t]], preferred_element_type=jnp.float32
        ).astype(jnp.bfloat16)
        term_image = lax.dot_general(
            left_part, right_ref[j], (((1,), (1,)), ((), ())),
            preferred_element_type=jnp.float32,
        )
        n_core, _, bands, band, _ = out_ref.shape
        target = tgt_ref[t]
        for q in range(bands):
            for cc in range(n_core):
                row = (q * n_core + cc) * band
                out_ref[cc, target, q] += term_image[row:row + band]


def add_terms(own, swapped, left_terms, right_terms, sources, targets, core, n_core, band):
    n_slab, width, _ = own.shape
    sectors = 2 * n_slab
    n_terms = left_terms.shape[0]
    out_shape = (n_core, sectors, width // (n_core * band), band, width)
    half = pl.BlockSpec((n_slab, width, width), lambda i, *_: (0, 0, 0))
    whole = pl.BlockSpec(out_shape, lambda i, *_: (0,) * len(out_shape))
    per_step = pl.BlockSpec((TERM_BLOCK, width, width), lambda i, *_: (i, 0, 0))
    return pl.pallas_call(
        sigma_kernel,
        out_shape=jax.ShapeDtypeStruct(out_shape, jnp.float32),
        grid_spec=pltpu.PrefetchScalarGridSpec(
            num_scalar_prefetch=3,
            grid=(n_terms // TERM_BLOCK,),
            in_specs=[half, half, per_step, per_step],
            out_specs=whole,
            scratch_shapes=[pltpu.VMEM((sectors, width, width), own.dtype)],
        ),
        compiler_params=pltpu.CompilerParams(dimension_semantics=("arbitrary",)),
    )(core, sources, targets, own, swapped, left_terms, right_terms)


def gather_blocks(wavefunction, n_blk):
    core = lax.axis_index("c")
    mine = lax.dynamic_index_in_dim(wavefunction, core, 0, keepdims=False)
    copies = jnp.broadcast_to(mine[None], (n_blk,) + mine.shape)
    own = lax.all_to_all(copies, ("y", "xh"), 0, 0, tiled=True)
    swapped = lax.ppermute(own, "c", [(0, 1), (1, 0)])
    return own, swapped


def on_device(wavefunction, left_terms, right_terms, term_slab, term_sector, term_target):
    per_slab = wavefunction.shape[0]
    n_blk = lax.axis_size(("y", "xh"))
    n_core = lax.axis_size("c")
    n_rest = lax.axis_size(("y", "xh", "z", "xl"))
    width = wavefunction.shape[1]
    band = per_slab * n_blk * width // (n_core * n_rest)
    sources = term_slab[:, 0] * per_slab + term_sector
    core = lax.axis_index("c").astype(jnp.int32).reshape(1)
    own, swapped = gather_blocks(wavefunction, n_blk)
    parts = add_terms(own, swapped, left_terms, right_terms, sources, term_target, core, n_core, band)
    mine = lax.dynamic_index_in_dim(parts, core[0], 0, keepdims=False).reshape(n_rest, band, width)
    other = lax.dynamic_index_in_dim(parts, 1 - core[0], 0, keepdims=False).reshape(n_rest, band, width)
    summed = mine + lax.ppermute(other, "c", [(0, 1), (1, 0)])
    got = lax.all_to_all(summed, ("y", "xh", "z", "xl"), 0, 0, tiled=True)
    return got.sum(0)


def solution(mesh):
    blk, terms = mesh.axis_names
    n_blk, n_terms = mesh.shape[blk], mesh.shape[terms]
    n_core = 2
    phys = Mesh(
        mesh.devices.reshape(n_blk // 2, 2, n_terms // (2 * n_core), 2, n_core), PHYS
    )
    wave = ("y", "xh")
    spread = PHYS
    placed = (
        P(wave, None, None),
        P(spread, None, None),
        P(spread, None, None),
        P(spread, None),
        P(spread),
        P(spread),
    )
    return jax.shard_map(
        on_device, mesh=phys, in_specs=placed, out_specs=P(spread, None), check_vma=False
    )
```

```python
import jax
import jax.numpy as jnp
from jax import lax
from jax.experimental import pallas as pl
from jax.experimental.pallas import tpu as pltpu
from jax.sharding import Mesh
from jax.sharding import PartitionSpec as P

PHYS = ("y", "xh", "z", "xl", "c")
TERM_BLOCK = 32


def sigma_kernel(core_ref, src_ref, tgt_ref, own_ref, swapped_ref, left_ref, right_ref,
                 mine_ref, other_ref, psi_ref):
    step = pl.program_id(0)

    @pl.when(step == 0)
    def _():
        core = core_ref[0]
        for b in range(own_ref.shape[0]):
            psi_ref[2 * b + core] = own_ref[b]
            psi_ref[2 * b + 1 - core] = swapped_ref[b]
        mine_ref[...] = jnp.zeros_like(mine_ref)
        other_ref[...] = jnp.zeros_like(other_ref)

    for j in range(TERM_BLOCK):
        t = step * TERM_BLOCK + j
        left_part = jnp.dot(
            left_ref[j], psi_ref[src_ref[t]], preferred_element_type=jnp.float32
        ).astype(jnp.bfloat16)
        term_image = lax.dot_general(
            left_part, right_ref[j], (((1,), (1,)), ((), ())),
            preferred_element_type=jnp.float32,
        )
        _, bands, band, _ = mine_ref.shape
        target = tgt_ref[t]
        first = core_ref[0] == 0
        for q in range(bands):
            low = term_image[2 * q * band:(2 * q + 1) * band]
            high = term_image[(2 * q + 1) * band:(2 * q + 2) * band]
            mine_ref[target, q] += jnp.where(first, low, high)
            other_ref[target, q] += jnp.where(first, high, low)


def add_terms(own, swapped, left_terms, right_terms, sources, targets, core, n_core, band):
    n_slab, width, _ = own.shape
    sectors = 2 * n_slab
    n_terms = left_terms.shape[0]
    out_shape = (sectors, width // (n_core * band), band, width)
    half = pl.BlockSpec((n_slab, width, width), lambda i, *_: (0, 0, 0))
    whole = pl.BlockSpec(out_shape, lambda i, *_: (0,) * len(out_shape))
    per_step = pl.BlockSpec((TERM_BLOCK, width, width), lambda i, *_: (i, 0, 0))
    return pl.pallas_call(
        sigma_kernel,
        out_shape=(jax.ShapeDtypeStruct(out_shape, jnp.float32),) * 2,
        grid_spec=pltpu.PrefetchScalarGridSpec(
            num_scalar_prefetch=3,
            grid=(n_terms // TERM_BLOCK,),
            in_specs=[half, half, per_step, per_step],
            out_specs=(whole, whole),
            scratch_shapes=[pltpu.VMEM((sectors, width, width), own.dtype)],
        ),
        compiler_params=pltpu.CompilerParams(dimension_semantics=("arbitrary",)),
    )(core, sources, targets, own, swapped, left_terms, right_terms)


def gather_blocks(wavefunction, n_blk):
    core = lax.axis_index("c")
    mine = lax.dynamic_index_in_dim(wavefunction, core, 0, keepdims=False)
    copies = jnp.broadcast_to(mine[None], (n_blk,) + mine.shape)
    own = lax.all_to_all(copies, ("y", "xh"), 0, 0, tiled=True)
    swapped = lax.ppermute(own, "c", [(0, 1), (1, 0)])
    return own, swapped


def on_device(wavefunction, left_terms, right_terms, term_slab, term_sector, term_target):
    per_slab = wavefunction.shape[0]
    n_blk = lax.axis_size(("y", "xh"))
    n_core = lax.axis_size("c")
    n_rest = lax.axis_size(("y", "xh", "z", "xl"))
    width = wavefunction.shape[1]
    band = per_slab * n_blk * width // (n_core * n_rest)
    sources = term_slab[:, 0] * per_slab + term_sector
    core = lax.axis_index("c").astype(jnp.int32).reshape(1)
    own, swapped = gather_blocks(wavefunction, n_blk)
    mine, other = add_terms(own, swapped, left_terms, right_terms, sources, term_target, core, n_core, band)
    mine = mine.reshape(n_rest, band, width)
    other = other.reshape(n_rest, band, width)
    summed = mine + lax.ppermute(other, "c", [(0, 1), (1, 0)])
    got = lax.all_to_all(summed, ("y", "xh", "z", "xl"), 0, 0, tiled=True)
    return got.sum(0)


def solution(mesh):
    blk, terms = mesh.axis_names
    n_blk, n_terms = mesh.shape[blk], mesh.shape[terms]
    n_core = 2
    phys = Mesh(
        mesh.devices.reshape(n_blk // 2, 2, n_terms // (2 * n_core), 2, n_core), PHYS
    )
    wave = ("y", "xh")
    spread = PHYS
    placed = (
        P(wave, None, None),
        P(spread, None, None),
        P(spread, None, None),
        P(spread, None),
        P(spread),
        P(spread),
    )
    return jax.shard_map(
        on_device, mesh=phys, in_specs=placed, out_specs=P(spread, None), check_vma=False
    )
```

```python
import jax
import jax.numpy as jnp
from jax import lax
from jax.experimental import pallas as pl
from jax.experimental.pallas import tpu as pltpu
from jax.sharding import Mesh
from jax.sharding import PartitionSpec as P

PHYS = ("y", "xh", "z", "xl", "c")
TERM_BLOCK = 32


def sigma_kernel(core_ref, slab_ref, sector_ref, tgt_ref, own_ref, swapped_ref, left_ref,
                 right_ref, mine_ref, other_ref):
    step = pl.program_id(0)

    @pl.when(step == 0)
    def _():
        mine_ref[...] = jnp.zeros_like(mine_ref)
        other_ref[...] = jnp.zeros_like(other_ref)

    for j in range(TERM_BLOCK):
        t = step * TERM_BLOCK + j
        slab = slab_ref[t]
        psi = jnp.where(sector_ref[t] == core_ref[0], own_ref[slab], swapped_ref[slab])
        left_part = jnp.dot(
            left_ref[j], psi, preferred_element_type=jnp.float32
        ).astype(jnp.bfloat16)
        term_image = lax.dot_general(
            left_part, right_ref[j], (((1,), (1,)), ((), ())),
            preferred_element_type=jnp.float32,
        )
        _, bands, band, _ = mine_ref.shape
        target = tgt_ref[t]
        first = core_ref[0] == 0
        for q in range(bands):
            low = term_image[2 * q * band:(2 * q + 1) * band]
            high = term_image[(2 * q + 1) * band:(2 * q + 2) * band]
            mine_ref[target, q] += jnp.where(first, low, high)
            other_ref[target, q] += jnp.where(first, high, low)


def add_terms(own, swapped, left_terms, right_terms, slab, sector, targets, core, n_core, band):
    n_slab, width, _ = own.shape
    sectors = 2 * n_slab
    n_terms = left_terms.shape[0]
    out_shape = (sectors, width // (n_core * band), band, width)
    half = pl.BlockSpec((n_slab, width, width), lambda i, *_: (0, 0, 0))
    whole = pl.BlockSpec(out_shape, lambda i, *_: (0,) * len(out_shape))
    per_step = pl.BlockSpec((TERM_BLOCK, width, width), lambda i, *_: (i, 0, 0))
    return pl.pallas_call(
        sigma_kernel,
        out_shape=(jax.ShapeDtypeStruct(out_shape, jnp.float32),) * 2,
        grid_spec=pltpu.PrefetchScalarGridSpec(
            num_scalar_prefetch=4,
            grid=(n_terms // TERM_BLOCK,),
            in_specs=[half, half, per_step, per_step],
            out_specs=(whole, whole),
        ),
        compiler_params=pltpu.CompilerParams(dimension_semantics=("arbitrary",)),
    )(core, slab, sector, targets, own, swapped, left_terms, right_terms)


def gather_blocks(wavefunction, n_blk):
    core = lax.axis_index("c")
    mine = lax.dynamic_index_in_dim(wavefunction, core, 0, keepdims=False)
    copies = jnp.broadcast_to(mine[None], (n_blk,) + mine.shape)
    own = lax.all_to_all(copies, ("y", "xh"), 0, 0, tiled=True)
    swapped = lax.ppermute(own, "c", [(0, 1), (1, 0)])
    return own, swapped


def on_device(wavefunction, left_terms, right_terms, term_slab, term_sector, term_target):
    per_slab = wavefunction.shape[0]
    n_blk = lax.axis_size(("y", "xh"))
    n_core = lax.axis_size("c")
    n_rest = lax.axis_size(("y", "xh", "z", "xl"))
    width = wavefunction.shape[1]
    band = per_slab * n_blk * width // (n_core * n_rest)
    core = lax.axis_index("c").astype(jnp.int32).reshape(1)
    own, swapped = gather_blocks(wavefunction, n_blk)
    mine, other = add_terms(
        own, swapped, left_terms, right_terms, term_slab[:, 0], term_sector, term_target,
        core, n_core, band,
    )
    mine = mine.reshape(n_rest, band, width)
    other = other.reshape(n_rest, band, width)
    summed = mine + lax.ppermute(other, "c", [(0, 1), (1, 0)])
    got = lax.all_to_all(summed, ("y", "xh", "z", "xl"), 0, 0, tiled=True)
    return got.sum(0)


def solution(mesh):
    blk, terms = mesh.axis_names
    n_blk, n_terms = mesh.shape[blk], mesh.shape[terms]
    n_core = 2
    phys = Mesh(
        mesh.devices.reshape(n_blk // 2, 2, n_terms // (2 * n_core), 2, n_core), PHYS
    )
    wave = ("y", "xh")
    spread = PHYS
    placed = (
        P(wave, None, None),
        P(spread, None, None),
        P(spread, None, None),
        P(spread, None),
        P(spread),
        P(spread),
    )
    return jax.shard_map(
        on_device, mesh=phys, in_specs=placed, out_specs=P(spread, None), check_vma=False
    )
```

```python
import jax
import jax.numpy as jnp
from jax import lax
from jax.experimental import pallas as pl
from jax.experimental.pallas import tpu as pltpu
from jax.sharding import Mesh
from jax.sharding import PartitionSpec as P

PHYS = ("y", "xh", "z", "xl", "c")
TERM_BLOCK = 16


def sigma_kernel(core_ref, src_ref, tgt_ref, own_ref, swapped_ref, left_ref, right_ref,
                 mine_ref, other_ref, psi_ref):
    step = pl.program_id(0)

    @pl.when(step == 0)
    def _():
        core = core_ref[0]
        for b in range(own_ref.shape[0]):
            psi_ref[2 * b + core] = own_ref[b]
            psi_ref[2 * b + 1 - core] = swapped_ref[b]
        mine_ref[...] = jnp.zeros_like(mine_ref)
        other_ref[...] = jnp.zeros_like(other_ref)

    for j in range(TERM_BLOCK):
        t = step * TERM_BLOCK + j
        left_part = jnp.dot(
            left_ref[j], psi_ref[src_ref[t]], preferred_element_type=jnp.float32
        ).astype(jnp.bfloat16)
        term_image = lax.dot_general(
            left_part, right_ref[j], (((1,), (1,)), ((), ())),
            preferred_element_type=jnp.float32,
        )
        _, bands, band, _ = mine_ref.shape
        target = tgt_ref[t]
        first = core_ref[0] == 0
        for q in range(bands):
            low = term_image[2 * q * band:(2 * q + 1) * band]
            high = term_image[(2 * q + 1) * band:(2 * q + 2) * band]
            mine_ref[target, q] += jnp.where(first, low, high)
            other_ref[target, q] += jnp.where(first, high, low)


def add_terms(own, swapped, left_terms, right_terms, sources, targets, core, n_core, band):
    n_slab, width, _ = own.shape
    sectors = 2 * n_slab
    n_terms = left_terms.shape[0]
    out_shape = (sectors, width // (n_core * band), band, width)
    half = pl.BlockSpec((n_slab, width, width), lambda i, *_: (0, 0, 0))
    whole = pl.BlockSpec(out_shape, lambda i, *_: (0,) * len(out_shape))
    per_step = pl.BlockSpec((TERM_BLOCK, width, width), lambda i, *_: (i, 0, 0))
    return pl.pallas_call(
        sigma_kernel,
        out_shape=(jax.ShapeDtypeStruct(out_shape, jnp.float32),) * 2,
        grid_spec=pltpu.PrefetchScalarGridSpec(
            num_scalar_prefetch=3,
            grid=(n_terms // TERM_BLOCK,),
            in_specs=[half, half, per_step, per_step],
            out_specs=(whole, whole),
            scratch_shapes=[pltpu.VMEM((sectors, width, width), own.dtype)],
        ),
        compiler_params=pltpu.CompilerParams(dimension_semantics=("arbitrary",)),
    )(core, sources, targets, own, swapped, left_terms, right_terms)


def gather_blocks(wavefunction, n_blk):
    core = lax.axis_index("c")
    mine = lax.dynamic_index_in_dim(wavefunction, core, 0, keepdims=False)
    copies = jnp.broadcast_to(mine[None], (n_blk,) + mine.shape)
    own = lax.all_to_all(copies, ("y", "xh"), 0, 0, tiled=True)
    swapped = lax.ppermute(own, "c", [(0, 1), (1, 0)])
    return own, swapped


def on_device(wavefunction, left_terms, right_terms, term_slab, term_sector, term_target):
    per_slab = wavefunction.shape[0]
    n_blk = lax.axis_size(("y", "xh"))
    n_core = lax.axis_size("c")
    n_rest = lax.axis_size(("y", "xh", "z", "xl"))
    width = wavefunction.shape[1]
    band = per_slab * n_blk * width // (n_core * n_rest)
    sources = term_slab[:, 0] * per_slab + term_sector
    core = lax.axis_index("c").astype(jnp.int32).reshape(1)
    own, swapped = gather_blocks(wavefunction, n_blk)
    mine, other = add_terms(own, swapped, left_terms, right_terms, sources, term_target, core, n_core, band)
    mine = mine.reshape(n_rest, band, width)
    other = other.reshape(n_rest, band, width)
    summed = mine + lax.ppermute(other, "c", [(0, 1), (1, 0)])
    got = lax.all_to_all(summed, ("y", "xh", "z", "xl"), 0, 0, tiled=True)
    return got.sum(0)


def solution(mesh):
    blk, terms = mesh.axis_names
    n_blk, n_terms = mesh.shape[blk], mesh.shape[terms]
    n_core = 2
    phys = Mesh(
        mesh.devices.reshape(n_blk // 2, 2, n_terms // (2 * n_core), 2, n_core), PHYS
    )
    wave = ("y", "xh")
    spread = PHYS
    placed = (
        P(wave, None, None),
        P(spread, None, None),
        P(spread, None, None),
        P(spread, None),
        P(spread),
        P(spread),
    )
    return jax.shard_map(
        on_device, mesh=phys, in_specs=placed, out_specs=P(spread, None), check_vma=False
    )
```

```python
import jax
import jax.numpy as jnp
from jax import lax
from jax.experimental import pallas as pl
from jax.experimental.pallas import tpu as pltpu
from jax.sharding import Mesh
from jax.sharding import PartitionSpec as P

PHYS = ("y", "xh", "z", "xl", "c")
TERM_BLOCK = 32


def sigma_kernel(core_ref, src_ref, tgt_ref, own_ref, swapped_ref, left_ref, right_ref,
                 mine_ref, other_ref, psi_ref):
    step = pl.program_id(0)

    @pl.when(step == 0)
    def _():
        core = core_ref[0]
        for b in range(own_ref.shape[0]):
            psi_ref[2 * b + core] = own_ref[b]
            psi_ref[2 * b + 1 - core] = swapped_ref[b]
        mine_ref[...] = jnp.zeros_like(mine_ref)
        other_ref[...] = jnp.zeros_like(other_ref)

    for j in range(TERM_BLOCK):
        t = step * TERM_BLOCK + j
        left_part = jnp.dot(
            left_ref[j], psi_ref[src_ref[t]], preferred_element_type=jnp.float32
        ).astype(jnp.bfloat16)
        term_image = lax.dot_general(
            left_part, right_ref[j], (((1,), (1,)), ((), ())),
            preferred_element_type=jnp.float32,
        )
        _, bands, band, _ = mine_ref.shape
        target = tgt_ref[t]
        first = core_ref[0] == 0
        for q in range(bands):
            low = term_image[2 * q * band:(2 * q + 1) * band]
            high = term_image[(2 * q + 1) * band:(2 * q + 2) * band]
            mine_ref[target, q] += jnp.where(first, low, high)
            other_ref[target, q] += jnp.where(first, high, low)


def add_terms(own, swapped, left_terms, right_terms, sources, targets, core, n_core, band):
    n_slab, width, _ = own.shape
    sectors = 2 * n_slab
    n_terms = left_terms.shape[0]
    out_shape = (sectors, width // (n_core * band), band, width)
    half = pl.BlockSpec((n_slab, width, width), lambda i, *_: (0, 0, 0))
    whole = pl.BlockSpec(out_shape, lambda i, *_: (0,) * len(out_shape))
    per_step = pl.BlockSpec((TERM_BLOCK, width, width), lambda i, *_: (i, 0, 0))
    return pl.pallas_call(
        sigma_kernel,
        out_shape=(jax.ShapeDtypeStruct(out_shape, jnp.float32),) * 2,
        grid_spec=pltpu.PrefetchScalarGridSpec(
            num_scalar_prefetch=3,
            grid=(n_terms // TERM_BLOCK,),
            in_specs=[half, half, per_step, per_step],
            out_specs=(whole, whole),
            scratch_shapes=[pltpu.VMEM((sectors, width, width), own.dtype)],
        ),
        compiler_params=pltpu.CompilerParams(dimension_semantics=("arbitrary",)),
    )(core, sources, targets, own, swapped, left_terms, right_terms)


def gather_blocks(wavefunction, n_blk):
    core = lax.axis_index("c")
    mine = lax.dynamic_index_in_dim(wavefunction, core, 0, keepdims=False)
    copies = jnp.broadcast_to(mine[None], (n_blk,) + mine.shape)
    own = lax.all_to_all(copies, ("y", "xh"), 0, 0, tiled=True)
    swapped = lax.ppermute(own, "c", [(0, 1), (1, 0)])
    return own, swapped


def on_device(wavefunction, left_terms, right_terms, term_slab, term_sector, term_target):
    per_slab = wavefunction.shape[0]
    n_blk = lax.axis_size(("y", "xh"))
    n_core = lax.axis_size("c")
    n_rest = lax.axis_size(("y", "xh", "z", "xl"))
    width = wavefunction.shape[1]
    band = per_slab * n_blk * width // (n_core * n_rest)
    sources = term_slab[:, 0] * per_slab + term_sector
    core = lax.axis_index("c").astype(jnp.int32).reshape(1)
    own, swapped = gather_blocks(wavefunction, n_blk)
    mine, other = add_terms(own, swapped, left_terms, right_terms, sources, term_target, core, n_core, band)
    mine = mine.reshape(n_rest, band, width)
    other = other.reshape(n_rest, band, width)
    half = n_rest // 2
    swap = [(0, 1), (1, 0)]
    first = lax.ppermute(other[:half], "c", swap)
    second = lax.ppermute(other[half:], "c", swap)
    summed = mine + jnp.concatenate([first, second], 0)
    got = lax.all_to_all(summed, ("y", "xh", "z", "xl"), 0, 0, tiled=True)
    return got.sum(0)


def solution(mesh):
    blk, terms = mesh.axis_names
    n_blk, n_terms = mesh.shape[blk], mesh.shape[terms]
    n_core = 2
    phys = Mesh(
        mesh.devices.reshape(n_blk // 2, 2, n_terms // (2 * n_core), 2, n_core), PHYS
    )
    wave = ("y", "xh")
    spread = PHYS
    placed = (
        P(wave, None, None),
        P(spread, None, None),
        P(spread, None, None),
        P(spread, None),
        P(spread),
        P(spread),
    )
    return jax.shard_map(
        on_device, mesh=phys, in_specs=placed, out_specs=P(spread, None), check_vma=False
    )
```

```python
import jax
import jax.numpy as jnp
from jax import lax
from jax.experimental import pallas as pl
from jax.experimental.pallas import tpu as pltpu
from jax.sharding import Mesh
from jax.sharding import PartitionSpec as P

PHYS = ("y", "xh", "z", "xl", "c")
TERM_BLOCK = 32


def sigma_kernel(core_ref, src_ref, tgt_ref, own_ref, swapped_ref, left_ref, right_ref,
                 mine_ref, other_lo_ref, other_hi_ref, psi_ref):
    step = pl.program_id(0)

    @pl.when(step == 0)
    def _():
        core = core_ref[0]
        for b in range(own_ref.shape[0]):
            psi_ref[2 * b + core] = own_ref[b]
            psi_ref[2 * b + 1 - core] = swapped_ref[b]
        mine_ref[...] = jnp.zeros_like(mine_ref)
        other_lo_ref[...] = jnp.zeros_like(other_lo_ref)
        other_hi_ref[...] = jnp.zeros_like(other_hi_ref)

    for j in range(TERM_BLOCK):
        t = step * TERM_BLOCK + j
        left_part = jnp.dot(
            left_ref[j], psi_ref[src_ref[t]], preferred_element_type=jnp.float32
        ).astype(jnp.bfloat16)
        term_image = lax.dot_general(
            left_part, right_ref[j], (((1,), (1,)), ((), ())),
            preferred_element_type=jnp.float32,
        )
        _, bands, band, _ = mine_ref.shape
        split = other_lo_ref.shape[1]
        target = tgt_ref[t]
        first = core_ref[0] == 0
        for q in range(bands):
            low = term_image[2 * q * band:(2 * q + 1) * band]
            high = term_image[(2 * q + 1) * band:(2 * q + 2) * band]
            mine_ref[target, q] += jnp.where(first, low, high)
            if q < split:
                other_lo_ref[target, q] += jnp.where(first, high, low)
            else:
                other_hi_ref[target, q - split] += jnp.where(first, high, low)


def add_terms(own, swapped, left_terms, right_terms, sources, targets, core, n_core, band):
    n_slab, width, _ = own.shape
    sectors = 2 * n_slab
    n_terms = left_terms.shape[0]
    bands = width // (n_core * band)
    out_shape = (sectors, bands, band, width)
    half_shape = (sectors, bands // 2, band, width)
    half = pl.BlockSpec((n_slab, width, width), lambda i, *_: (0, 0, 0))
    whole = pl.BlockSpec(out_shape, lambda i, *_: (0,) * len(out_shape))
    halves = pl.BlockSpec(half_shape, lambda i, *_: (0,) * len(half_shape))
    per_step = pl.BlockSpec((TERM_BLOCK, width, width), lambda i, *_: (i, 0, 0))
    return pl.pallas_call(
        sigma_kernel,
        out_shape=(
            jax.ShapeDtypeStruct(out_shape, jnp.float32),
            jax.ShapeDtypeStruct(half_shape, jnp.float32),
            jax.ShapeDtypeStruct(half_shape, jnp.float32),
        ),
        grid_spec=pltpu.PrefetchScalarGridSpec(
            num_scalar_prefetch=3,
            grid=(n_terms // TERM_BLOCK,),
            in_specs=[half, half, per_step, per_step],
            out_specs=(whole, halves, halves),
            scratch_shapes=[pltpu.VMEM((sectors, width, width), own.dtype)],
        ),
        compiler_params=pltpu.CompilerParams(dimension_semantics=("arbitrary",)),
    )(core, sources, targets, own, swapped, left_terms, right_terms)


def gather_blocks(wavefunction, n_blk):
    core = lax.axis_index("c")
    mine = lax.dynamic_index_in_dim(wavefunction, core, 0, keepdims=False)
    copies = jnp.broadcast_to(mine[None], (n_blk,) + mine.shape)
    own = lax.all_to_all(copies, ("y", "xh"), 0, 0, tiled=True)
    swapped = lax.ppermute(own, "c", [(0, 1), (1, 0)])
    return own, swapped


def on_device(wavefunction, left_terms, right_terms, term_slab, term_sector, term_target):
    per_slab = wavefunction.shape[0]
    n_blk = lax.axis_size(("y", "xh"))
    n_core = lax.axis_size("c")
    n_rest = lax.axis_size(("y", "xh", "z", "xl"))
    width = wavefunction.shape[1]
    band = per_slab * n_blk * width // (n_core * n_rest)
    sources = term_slab[:, 0] * per_slab + term_sector
    core = lax.axis_index("c").astype(jnp.int32).reshape(1)
    own, swapped = gather_blocks(wavefunction, n_blk)
    mine, other_lo, other_hi = add_terms(
        own, swapped, left_terms, right_terms, sources, term_target, core, n_core, band
    )
    swap = [(0, 1), (1, 0)]
    received = jnp.concatenate(
        [lax.ppermute(other_lo, "c", swap), lax.ppermute(other_hi, "c", swap)], 1
    )
    summed = (mine + received).reshape(n_rest, band, width)
    got = lax.all_to_all(summed, ("y", "xh", "z", "xl"), 0, 0, tiled=True)
    return got.sum(0)


def solution(mesh):
    blk, terms = mesh.axis_names
    n_blk, n_terms = mesh.shape[blk], mesh.shape[terms]
    n_core = 2
    phys = Mesh(
        mesh.devices.reshape(n_blk // 2, 2, n_terms // (2 * n_core), 2, n_core), PHYS
    )
    wave = ("y", "xh")
    spread = PHYS
    placed = (
        P(wave, None, None),
        P(spread, None, None),
        P(spread, None, None),
        P(spread, None),
        P(spread),
        P(spread),
    )
    return jax.shard_map(
        on_device, mesh=phys, in_specs=placed, out_specs=P(spread, None), check_vma=False
    )
```

```python
import jax
import jax.numpy as jnp
from jax import lax
from jax.experimental import pallas as pl
from jax.experimental.pallas import tpu as pltpu
from jax.sharding import Mesh
from jax.sharding import PartitionSpec as P

PHYS = ("y", "xh", "z", "xl", "c")
TERM_BLOCK = 32


def sigma_kernel(core_ref, src_ref, tgt_ref, own_ref, swapped_ref, left_ref, right_ref,
                 mine_ref, other_ref, psi_ref):
    step = pl.program_id(0)

    @pl.when(step == 0)
    def _():
        core = core_ref[0]
        for b in range(own_ref.shape[0]):
            psi_ref[2 * b + core] = own_ref[b]
            psi_ref[2 * b + 1 - core] = swapped_ref[b]
        mine_ref[...] = jnp.zeros_like(mine_ref)
        other_ref[...] = jnp.zeros_like(other_ref)

    for j in range(TERM_BLOCK):
        t = step * TERM_BLOCK + j
        left_part = jnp.dot(
            left_ref[j], psi_ref[src_ref[t]], preferred_element_type=jnp.float32
        ).astype(jnp.bfloat16)
        term_image = lax.dot_general(
            left_part, right_ref[j], (((1,), (1,)), ((), ())),
            preferred_element_type=jnp.float32,
        )
        _, bands, band, _ = mine_ref.shape
        target = tgt_ref[t]
        first = core_ref[0] == 0
        for q in range(bands):
            low = term_image[2 * q * band:(2 * q + 1) * band]
            high = term_image[(2 * q + 1) * band:(2 * q + 2) * band]
            mine_ref[target, q] += jnp.where(first, low, high)
            other_ref[target, q] += jnp.where(first, high, low)


def add_terms(own, swapped, left_terms, right_terms, sources, targets, core, n_core, band):
    n_slab, width, _ = own.shape
    sectors = 2 * n_slab
    n_terms = left_terms.shape[0]
    out_shape = (sectors, width // (n_core * band), band, width)
    half = pl.BlockSpec((n_slab, width, width), lambda i, *_: (0, 0, 0))
    whole = pl.BlockSpec(out_shape, lambda i, *_: (0,) * len(out_shape))
    per_step = pl.BlockSpec((TERM_BLOCK, width, width), lambda i, *_: (i, 0, 0))
    return pl.pallas_call(
        sigma_kernel,
        out_shape=(jax.ShapeDtypeStruct(out_shape, jnp.float32),) * 2,
        grid_spec=pltpu.PrefetchScalarGridSpec(
            num_scalar_prefetch=3,
            grid=(n_terms // TERM_BLOCK,),
            in_specs=[half, half, per_step, per_step],
            out_specs=(whole, whole),
            scratch_shapes=[pltpu.VMEM((sectors, width, width), own.dtype)],
        ),
        compiler_params=pltpu.CompilerParams(dimension_semantics=("arbitrary",)),
    )(core, sources, targets, own, swapped, left_terms, right_terms)


def gather_blocks(wavefunction, n_blk):
    core = lax.axis_index("c")
    mine = lax.dynamic_index_in_dim(wavefunction, core, 0, keepdims=False)
    copies = jnp.broadcast_to(mine[None], (n_blk,) + mine.shape)
    own = lax.all_to_all(copies, ("y", "xh"), 0, 0, tiled=True)
    swapped = lax.ppermute(own, "c", [(0, 1), (1, 0)])
    return own, swapped


def on_device(wavefunction, left_terms, right_terms, term_slab, term_sector, term_target):
    per_slab = wavefunction.shape[0]
    n_blk = lax.axis_size(("y", "xh"))
    n_core = lax.axis_size("c")
    n_rest = lax.axis_size(("y", "xh", "z", "xl"))
    width = wavefunction.shape[1]
    band = per_slab * n_blk * width // (n_core * n_rest)
    sources = term_slab[:, 0] * per_slab + term_sector
    core = lax.axis_index("c").astype(jnp.int32).reshape(1)
    own, swapped = gather_blocks(wavefunction, n_blk)
    mine, other = add_terms(own, swapped, left_terms, right_terms, sources, term_target, core, n_core, band)
    mine = mine.reshape(n_rest, band, width)
    mine = lax.optimization_barrier(jnp.where(mine == mine, mine, 0.0))
    other = other.reshape(n_rest, band, width)
    summed = mine + lax.ppermute(other, "c", [(0, 1), (1, 0)])
    got = lax.all_to_all(summed, ("y", "xh", "z", "xl"), 0, 0, tiled=True)
    return got.sum(0)


def solution(mesh):
    blk, terms = mesh.axis_names
    n_blk, n_terms = mesh.shape[blk], mesh.shape[terms]
    n_core = 2
    phys = Mesh(
        mesh.devices.reshape(n_blk // 2, 2, n_terms // (2 * n_core), 2, n_core), PHYS
    )
    wave = ("y", "xh")
    spread = PHYS
    placed = (
        P(wave, None, None),
        P(spread, None, None),
        P(spread, None, None),
        P(spread, None),
        P(spread),
        P(spread),
    )
    return jax.shard_map(
        on_device, mesh=phys, in_specs=placed, out_specs=P(spread, None), check_vma=False
    )
```

```python
import jax
import jax.numpy as jnp
from jax import lax
from jax.experimental import pallas as pl
from jax.experimental.pallas import tpu as pltpu
from jax.sharding import Mesh
from jax.sharding import PartitionSpec as P

PHYS = ("y", "xh", "z", "xl", "c")
TERM_BLOCK = 32


def sigma_kernel(core_ref, src_ref, tgt_ref, own_ref, swapped_ref, left_ref, right_ref,
                 mine_ref, other_ref, psi_ref):
    step = pl.program_id(0)

    @pl.when(step == 0)
    def _():
        core = core_ref[0]
        for b in range(own_ref.shape[0]):
            psi_ref[2 * b + core] = own_ref[b]
            psi_ref[2 * b + 1 - core] = swapped_ref[b]
        mine_ref[...] = jnp.zeros_like(mine_ref)
        other_ref[...] = jnp.zeros_like(other_ref)

    for j in range(TERM_BLOCK):
        t = step * TERM_BLOCK + j
        left_part = jnp.dot(
            left_ref[j], psi_ref[src_ref[t]], preferred_element_type=jnp.float32
        ).astype(jnp.bfloat16)
        term_image = lax.dot_general(
            left_part, right_ref[j], (((1,), (1,)), ((), ())),
            preferred_element_type=jnp.float32,
        )
        _, bands, band, _ = mine_ref.shape
        target = tgt_ref[t]
        first = core_ref[0] == 0
        for q in range(bands):
            low = term_image[2 * q * band:(2 * q + 1) * band]
            high = term_image[(2 * q + 1) * band:(2 * q + 2) * band]
            mine_ref[target, q] += jnp.where(first, low, high)
            other_ref[target, q] += jnp.where(first, high, low)


def add_terms(own, swapped, left_terms, right_terms, sources, targets, core, n_core, band):
    n_slab, width, _ = own.shape
    sectors = 2 * n_slab
    n_terms = left_terms.shape[0]
    out_shape = (sectors, width // (n_core * band), band, width)
    half = pl.BlockSpec((n_slab, width, width), lambda i, *_: (0, 0, 0))
    whole = pl.BlockSpec(out_shape, lambda i, *_: (0,) * len(out_shape))
    per_step = pl.BlockSpec((TERM_BLOCK, width, width), lambda i, *_: (i, 0, 0))
    return pl.pallas_call(
        sigma_kernel,
        out_shape=(jax.ShapeDtypeStruct(out_shape, jnp.float32),) * 2,
        grid_spec=pltpu.PrefetchScalarGridSpec(
            num_scalar_prefetch=3,
            grid=(n_terms // TERM_BLOCK,),
            in_specs=[half, half, per_step, per_step],
            out_specs=(whole, whole),
            scratch_shapes=[pltpu.VMEM((sectors, width, width), own.dtype)],
        ),
        compiler_params=pltpu.CompilerParams(dimension_semantics=("arbitrary",)),
    )(core, sources, targets, own, swapped, left_terms, right_terms)


def gather_blocks(wavefunction, n_blk):
    core = lax.axis_index("c")
    mine = jnp.where(core == 0, wavefunction[0], wavefunction[1])
    copies = jnp.broadcast_to(mine[None], (n_blk,) + mine.shape)
    own = lax.all_to_all(copies, ("y", "xh"), 0, 0, tiled=True)
    swapped = lax.ppermute(own, "c", [(0, 1), (1, 0)])
    return own, swapped


def on_device(wavefunction, left_terms, right_terms, term_slab, term_sector, term_target):
    per_slab = wavefunction.shape[0]
    n_blk = lax.axis_size(("y", "xh"))
    n_core = lax.axis_size("c")
    n_rest = lax.axis_size(("y", "xh", "z", "xl"))
    width = wavefunction.shape[1]
    band = per_slab * n_blk * width // (n_core * n_rest)
    sources = term_slab[:, 0] * per_slab + term_sector
    core = lax.axis_index("c").astype(jnp.int32).reshape(1)
    own, swapped = gather_blocks(wavefunction, n_blk)
    mine, other = add_terms(own, swapped, left_terms, right_terms, sources, term_target, core, n_core, band)
    mine = mine.reshape(n_rest, band, width)
    mine = lax.optimization_barrier(jnp.where(mine == mine, mine, 0.0))
    other = other.reshape(n_rest, band, width)
    summed = mine + lax.ppermute(other, "c", [(0, 1), (1, 0)])
    got = lax.all_to_all(summed, ("y", "xh", "z", "xl"), 0, 0, tiled=True)
    return got.sum(0)


def solution(mesh):
    blk, terms = mesh.axis_names
    n_blk, n_terms = mesh.shape[blk], mesh.shape[terms]
    n_core = 2
    phys = Mesh(
        mesh.devices.reshape(n_blk // 2, 2, n_terms // (2 * n_core), 2, n_core), PHYS
    )
    wave = ("y", "xh")
    spread = PHYS
    placed = (
        P(wave, None, None),
        P(spread, None, None),
        P(spread, None, None),
        P(spread, None),
        P(spread),
        P(spread),
    )
    return jax.shard_map(
        on_device, mesh=phys, in_specs=placed, out_specs=P(spread, None), check_vma=False
    )
```
